32 devices in a mesh: ctx: 8 (over z, y), grp: 4 (over x, core).
Axes of the slice: x: 2, y: 2, z: 4, core: 2. Of those that a mesh axis runs over, the one named last changes fastest.
Arguments:
- query: bfloat16 [1024, 12288], P('ctx', 'grp')
- land_keys: bfloat16 [32, 768], P('ctx')
- land_values: bfloat16 [32, 512], P('ctx'), may hold values from -6 to 6
- d_out: bfloat16 [1024, 8192], P('ctx', 'grp'), may hold values from -6 to 6
- doc_start: int32 [1024], P('ctx'), may hold values from 0 to 1023, as said below
Outputs:
- branch_out: bfloat16 [1024, 8192], P('ctx', 'grp')
- d_query: float32 [1024, 12288], P('ctx', 'grp')
- d_keys: float32 [32, 768], P('ctx')
- d_values: float32 [32, 512], P('ctx')
The draws below stay inside these ranges and needn't reach their ends.
Inputs may be any that keep to these rules, and one draw needn't show every extreme that they name: doc_start never decreases from one position to the next, doc_start[t] <= t, a document starts at position 0, and one starts at the last position.
All inputs are finite; a program needn't handle non-finite values.
Results may differ from the reference program's by a relative error of at most 0.0049.
Values may be sent and summed in bfloat16 or wider, within the bound.
No kernel may reach another device: no remote copies, remote signals or barrier semaphores. Data moves between devices by JAX's collectives and lax.ppermute only.
A program may use at most 64 MiB of HBM per device.

```python
import math
import jax
import jax.numpy as jnp
from jax import lax

HEADS = 64
KVG = 4
DK = 192
DV = 128
BLK = 32
DOC_LEN = 2048
TOKENS = 1024
NL = 32


def landmark_base(key):
    return jax.random.normal(jax.random.fold_in(key, 11), (NL, KVG * DK), jnp.float32)


def draw_land_keys(key, part):
    return landmark_base(key).astype(jnp.bfloat16)


def draw_query(key, part):
    drawn = jax.random.normal(jax.random.fold_in(key, 12), (TOKENS, HEADS, DK), jnp.float32)
    return drawn.reshape(TOKENS, HEADS * DK).astype(jnp.bfloat16)


def draw_doc_start(key, part):
    positions = jnp.arange(TOKENS, dtype=jnp.int32)
    marks = jax.random.randint(jax.random.fold_in(key, 13), (TOKENS,), 0, DOC_LEN) == 0
    marks = marks | (positions == 0) | (positions == TOKENS - 1)
    return lax.cummax(jnp.where(marks, positions, 0), axis=0).astype(jnp.int32)


def level_of(stream_key, extent, pieces, smallest, largest):
    factor_of, own = 1.0, jax.random.fold_in(stream_key, 6)
    for position, parts in pieces:
        draws = jnp.exp(jax.random.uniform(jax.random.fold_in(own, position), (parts,), jnp.float32, smallest / len(pieces), largest / len(pieces)))
        factor_of = factor_of * jnp.repeat(draws, extent[position] // parts).reshape([-1 if axis == position else 1 for axis in range(len(extent))])
    return factor_of


def centred(own_key, extent, width, limit, cuts=(), kind=jnp.bfloat16):
    loudness = level_of(own_key, extent, cuts, -0.22, 0.18) if cuts else 1.0
    entries = jax.random.normal(own_key, extent, jnp.float32) * width * loudness
    return jnp.minimum(jnp.maximum(entries, -limit), limit).astype(kind)


def setup_inputs(seed: int = 0) -> dict:
    key_of = jax.random.split(jax.random.key(seed), 6)
    return {
        "query": draw_query(jax.random.fold_in(key_of[5], 71), 0),
        "land_keys": draw_land_keys(jax.random.fold_in(key_of[5], 71), 0),
        "land_values": centred(key_of[2], (NL, KVG * DV), 1.0, 6.0, ((0, 8),)),
        "d_out": centred(key_of[3], (TOKENS, HEADS * DV), 1.0, 6.0, ((0, 8), (1, 4))),
        "doc_start": draw_doc_start(jax.random.fold_in(key_of[5], 71), 0),
    }


def reference(query, land_keys, land_values, d_out, doc_start):
    score_scale = 1.0 / math.sqrt(DK)
    positions = jnp.arange(TOKENS, dtype=jnp.int32)
    landmark_ids = jnp.arange(NL, dtype=jnp.int32)
    allowed = (landmark_ids[None, :] * BLK >= doc_start[:, None]) & ((landmark_ids[None, :] + 1) * BLK <= positions[:, None] + 1)
    queries = query.reshape(TOKENS, HEADS, DK)
    grads_in = d_out.reshape(TOKENS, HEADS, DV)
    keys_all = land_keys.reshape(NL, KVG, DK)
    values_all = land_values.reshape(NL, KVG, DV)
    per_group = HEADS // KVG

    def one_head(carry, head_index):
        group = head_index // per_group
        q_head = lax.dynamic_index_in_dim(queries, head_index, 1, keepdims=False)
        g_head = lax.dynamic_index_in_dim(grads_in, head_index, 1, keepdims=False)
        k_head = lax.dynamic_index_in_dim(keys_all, group, 1, keepdims=False)
        v_head = lax.dynamic_index_in_dim(values_all, group, 1, keepdims=False)
        scores = jnp.dot(q_head, k_head.T, preferred_element_type=jnp.float32) * score_scale
        masked = jnp.where(allowed, scores, -1e+30)
        peak = jnp.maximum(lax.optimization_barrier(jnp.max(masked, axis=1)), 0.0)
        expo = jnp.where(allowed, jnp.exp(masked - peak[:, None]), 0.0)
        denom = jnp.exp(-peak) + lax.optimization_barrier(jnp.sum(expo, axis=1))
        weight = expo / denom[:, None]
        weight_b = weight.astype(jnp.bfloat16)
        context = jnp.dot(weight_b, v_head, preferred_element_type=jnp.float32)
        delta = lax.optimization_barrier(jnp.sum(g_head.astype(jnp.float32) * context, axis=1))
        d_weight = jnp.dot(g_head, v_head.T, preferred_element_type=jnp.float32)
        d_score = weight * (d_weight - delta[:, None])
        d_score_b = d_score.astype(jnp.bfloat16)
        dq_head = jnp.dot(d_score_b, k_head, preferred_element_type=jnp.float32) * score_scale
        dk_head = jnp.dot(d_score_b.T, q_head, preferred_element_type=jnp.float32) * score_scale
        dv_head = jnp.dot(weight_b.T, g_head, preferred_element_type=jnp.float32)
        dk_acc, dv_acc = carry
        dk_acc = lax.dynamic_update_index_in_dim(dk_acc, lax.dynamic_index_in_dim(dk_acc, group, 1, keepdims=False) + dk_head, group, 1)
        dv_acc = lax.dynamic_update_index_in_dim(dv_acc, lax.dynamic_index_in_dim(dv_acc, group, 1, keepdims=False) + dv_head, group, 1)
        return ((dk_acc, dv_acc), (context.astype(jnp.bfloat16), dq_head))
    start_carry = (jnp.zeros((NL, KVG, DK), jnp.float32), jnp.zeros((NL, KVG, DV), jnp.float32))
    (dk_acc, dv_acc), (contexts, dq_all) = lax.scan(one_head, start_carry, jnp.arange(HEADS, dtype=jnp.int32))
    branch_out = jnp.transpose(contexts, (1, 0, 2)).reshape(TOKENS, HEADS * DV)
    d_query = jnp.transpose(dq_all, (1, 0, 2)).reshape(TOKENS, HEADS * DK)
    return (branch_out, d_query, dk_acc.reshape(NL, KVG * DK), dv_acc.reshape(NL, KVG * DV))
```

```python
import math

import jax
import jax.numpy as jnp
from jax import lax
from jax.sharding import PartitionSpec as P

KVG = 4
DK = 192
DV = 128
BLK = 32


def gather_ctx(block):
    n = lax.axis_size("ctx")
    if n & (n - 1):
        return lax.all_gather(block, "ctx", axis=0, tiled=True)
    copies = jnp.broadcast_to(block[None], (n,) + block.shape)
    return lax.all_to_all(copies, "ctx", 0, 0, tiled=False).reshape(n * block.shape[0], block.shape[1])


def shards(query, land_keys, land_values, d_out, doc_start):
    tok_rows = query.shape[0]
    head_count = query.shape[1] // DK
    nl_local = land_keys.shape[0]
    n_ctx = lax.axis_size("ctx")
    n_grp = lax.axis_size("grp")
    per_group = n_grp // KVG
    score_scale = 1.0 / math.sqrt(DK)
    group_id = lax.axis_index("grp") // per_group
    group_keys = lax.dynamic_slice_in_dim(land_keys, group_id * DK, DK, 1)
    group_values = lax.dynamic_slice_in_dim(land_values, group_id * DV, DV, 1)
    queries = query.reshape(tok_rows, head_count, DK)
    grads_in = d_out.reshape(tok_rows, head_count, DV)
    ctx_index = lax.axis_index("ctx")
    positions = ctx_index * tok_rows + jnp.arange(tok_rows, dtype=jnp.int32)
    landmarks = gather_ctx(jnp.concatenate([group_keys, group_values], axis=1))
    keys_whole, values_whole = landmarks[:, :DK], landmarks[:, DK:]
    columns = jnp.arange(keys_whole.shape[0], dtype=jnp.int32)
    allowed = (columns[None, :] * BLK >= doc_start[:, None]) & (
        (columns[None, :] + 1) * BLK <= positions[:, None] + 1
    )
    scores = (
        jnp.einsum("thd,jd->thj", queries, keys_whole, preferred_element_type=jnp.float32)
        * score_scale
    )
    masked, allowed = (jnp.where(allowed[:, None, :], scores, -1e30), allowed[:, None, :])
    peak = jnp.maximum(jnp.max(masked, axis=2), 0.0)
    expo = jnp.where(allowed, jnp.exp(masked - peak[..., None]), 0.0)
    denom = jnp.exp(-peak) + jnp.sum(expo, axis=2)
    weight = expo / denom[..., None]
    weight_b = weight.astype(jnp.bfloat16)
    context = jnp.einsum("thj,je->the", weight_b, values_whole, preferred_element_type=jnp.float32)
    branch_out = context.astype(jnp.bfloat16).reshape(tok_rows, head_count * DV)
    delta = jnp.sum(grads_in.astype(jnp.float32) * context, axis=2)
    d_weight = jnp.einsum("the,je->thj", grads_in, values_whole, preferred_element_type=jnp.float32)
    d_score_b = (weight * (d_weight - delta[..., None])).astype(jnp.bfloat16)
    d_query = (
        jnp.einsum("thj,jd->thd", d_score_b, keys_whole, preferred_element_type=jnp.float32)
        * score_scale
    ).reshape(tok_rows, head_count * DK)
    key_grad = (
        jnp.einsum("thj,thd->jd", d_score_b, queries, preferred_element_type=jnp.float32)
        * score_scale
    )
    value_grad = jnp.einsum("thj,the->je", weight_b, grads_in, preferred_element_type=jnp.float32)
    partial = jnp.concatenate([key_grad, value_grad], axis=1).reshape(1, n_ctx, nl_local, DK + DV)
    outgoing = jnp.broadcast_to(partial, (n_grp, n_ctx, nl_local, DK + DV)).reshape(
        n_grp * n_ctx, nl_local, DK + DV
    )
    incoming = lax.all_to_all(outgoing, ("grp", "ctx"), 0, 0, tiled=False)
    totals = incoming.reshape(KVG, per_group, n_ctx, nl_local, DK + DV).sum(axis=(1, 2))
    totals = jnp.transpose(totals, (1, 0, 2))
    d_keys = totals[:, :, :DK].reshape(nl_local, KVG * DK)
    d_values = totals[:, :, DK:].reshape(nl_local, KVG * DV)
    return (branch_out, d_query, d_keys, d_values)


def solution(mesh):
    return jax.shard_map(
        shards,
        mesh=mesh,
        in_specs=(P("ctx", "grp"), P("ctx", None), P("ctx", None), P("ctx", "grp"), P("ctx")),
        out_specs=(P("ctx", "grp"), P("ctx", "grp"), P("ctx", None), P("ctx", None)),
        check_vma=False,
    )
```
